512 devices in a mesh: section: 32 (over z_hi, y, core), tp: 16 (over z_lo, x).
Axes of the slice: x: 4, y: 4, z: 16 (z_hi: 4, z_lo: 4; z = z_hi * 4 + z_lo), core: 2. Of those that a mesh axis runs over, the one named last changes fastest.
Arguments:
- grad_in: bfloat16 [32, 160, 8192], P('section', None, 'tp'), may hold values from -6 to 6
- out_proj: bfloat16 [32, 4096, 8192], P('section', 'tp'), may hold values from -0.09375 to 0.09375
- value_proj: bfloat16 [32, 8192, 512], P('section', 'tp'), may hold values from -0.0625 to 0.0625
- head_delta: bfloat16 [32, 160, 4096], P('section', None, 'tp'), may hold values from -6 to 6
- pattern: bfloat16 [32, 32, 160, 160], P('section', 'tp'), may hold values from 0 to 0.25
- positions: int32 [160], replicated, may hold values from -1 to 31, as said below
- node_map: int32 [32, 32], P('section'), may hold values from 0 to 31, each once within a row
Outputs:
- residual_grad: bfloat16 [32, 160, 8192], P('section', None, 'tp')
- edge_scores: float32 [32, 32, 32], P('section')
The draws below stay inside these ranges and needn't reach their ends.
Inputs may be any that keep to these rules, and one draw needn't show every extreme that they name: positions[t] = (t mod 32) - p, or -1 where that is negative, with one left padding p of 0 to 15 for each block of 32 tokens; the first block is unpadded. `node_map`: each row names every node once.
All inputs are finite; a program needn't handle non-finite values.
Results may differ from the reference program's by a relative error of at most 0.0095.
Values may be sent and summed in bfloat16 or wider, within the bound.
No kernel may reach another device: no remote copies, remote signals or barrier semaphores. Data moves between devices by JAX's collectives and lax.ppermute only.
A program may use at most 128 MiB of HBM per device.

```python
import jax
import jax.numpy as jnp
from jax import lax

D = 8192
HEADS = 32
HEAD_DIM = 128
KV = 4
IG_STEPS = 5
PROMPT = 32
GROUP = 8
TOKENS = 160
LAYERS = 32


def draw_positions(key, part):
    padding = jax.random.randint(key, (IG_STEPS,), 0, PROMPT // 2)
    step_ids = jnp.arange(IG_STEPS)
    padding = jnp.where(step_ids == 0, 0, jnp.where(step_ids == 1, jnp.maximum(padding, 1), padding))
    token_ids = jnp.arange(TOKENS)
    shifted = token_ids % PROMPT - padding[token_ids // PROMPT]
    return jnp.maximum(shifted, -1).astype(jnp.int32)


def block_scale(rng, extent, cuts, smallest, high):
    factor_of = 1.0
    for axis_at, shards_of in cuts:
        steps = jax.random.uniform(jax.random.fold_in(jax.random.fold_in(rng, 6), axis_at), (shards_of,), jnp.float32, smallest / len(cuts), high / len(cuts))
        factor_of = factor_of * jnp.repeat(jnp.exp(steps), extent[axis_at] // shards_of).reshape((-1,) + (1,) * (len(extent) - 1 - axis_at))
    return factor_of


def centred(own_key, shape, spread, limit, cuts=(), held_as=jnp.bfloat16):
    factor_of = block_scale(own_key, shape, cuts, -0.22, 0.18) if cuts else 1.0
    array = jax.random.normal(own_key, shape, jnp.float32) * spread * factor_of
    return jnp.minimum(jnp.maximum(array, -limit), limit).astype(held_as)


def setup_inputs(seed: int = 0) -> dict:
    seeds = jax.random.split(jax.random.key(seed), 8)
    return {
        "grad_in": centred(seeds[0], (LAYERS, TOKENS, D), 1.0, 6.0, ((0, 32), (2, 16))),
        "out_proj": centred(seeds[1], (LAYERS, HEADS * HEAD_DIM, D), (HEADS * HEAD_DIM) ** -0.5, 0.09375, ((0, 32), (1, 16))),
        "value_proj": centred(seeds[2], (LAYERS, D, KV * HEAD_DIM), D ** -0.5, 0.0625, ((0, 32), (1, 16))),
        "head_delta": centred(seeds[3], (LAYERS, TOKENS, HEADS * HEAD_DIM), 1.0, 6.0, ((0, 32), (2, 16))),
        "pattern": jnp.clip(0.25 * jax.random.uniform(seeds[4], (LAYERS, HEADS, TOKENS, TOKENS), jnp.float32) ** block_scale(seeds[4], (LAYERS, HEADS, TOKENS, TOKENS), ((0, 32), (1, 16)), -0.2, 0.2), 0.0, 0.25).astype(jnp.bfloat16),
        "positions": draw_positions(jax.random.fold_in(seeds[7], 71), 0),
        "node_map": jax.vmap(lambda own: jax.random.permutation(own, HEADS))(jax.random.split(seeds[6], LAYERS)).reshape((LAYERS, HEADS)).astype(jnp.int32),
    }


def visible_mask(positions):
    token_ids = jnp.arange(TOKENS)
    block_ids = token_ids // PROMPT
    same_block = block_ids[:, None] == block_ids[None, :]
    allowed = same_block & (positions[None, :] >= 0) & (positions[None, :] <= positions[:, None])
    return allowed.astype(jnp.bfloat16)


def layer_backward(grad_rows, out_rows, value_rows, weights, visible):
    head_grad = jnp.dot(grad_rows, out_rows.T, preferred_element_type=jnp.float32).astype(jnp.bfloat16)
    masked = (weights * visible[None]).astype(jnp.float32)
    shaped = head_grad.astype(jnp.float32).reshape(TOKENS, HEADS, HEAD_DIM)
    value_grad = jnp.einsum("hts,thc->shc", masked, shaped).astype(jnp.bfloat16)
    group_grad = value_grad.astype(jnp.float32).reshape(TOKENS, KV, GROUP, HEAD_DIM).sum(axis=2)
    group_grad = group_grad.reshape(TOKENS, KV * HEAD_DIM).astype(jnp.bfloat16)
    increment = jnp.dot(group_grad, value_rows.T, preferred_element_type=jnp.float32)
    residual = (grad_rows.astype(jnp.float32) + increment).astype(jnp.bfloat16)
    return residual, increment.astype(jnp.bfloat16)


def reference(grad_in, out_proj, value_proj, head_delta, pattern, positions, node_map):
    visible = visible_mask(positions)

    def backward_one(inputs):
        grad_rows, out_rows, value_rows, weights = inputs
        return layer_backward(grad_rows, out_rows, value_rows, weights, visible)

    residual_grad, target_rows = lax.map(backward_one, (grad_in, out_proj, value_proj, pattern))
    flat_rows = target_rows.reshape(LAYERS, TOKENS * D)

    def score_one(inputs):
        delta_cols, out_rows, node_row, layer = inputs
        delta = jnp.einsum("thc,hcd->htd", delta_cols.astype(jnp.float32).reshape(TOKENS, HEADS, HEAD_DIM), out_rows.astype(jnp.float32).reshape(HEADS, HEAD_DIM, D)).astype(jnp.bfloat16)
        raw = jnp.dot(delta.reshape(HEADS, TOKENS * D), flat_rows.T, preferred_element_type=jnp.float32)
        later = jnp.arange(LAYERS) > layer
        raw = jnp.where(later[None, :], raw / TOKENS, jnp.zeros_like(raw))
        onehot = (node_row[:, None] == jnp.arange(HEADS)[None, :]).astype(jnp.float32)
        return jnp.dot(onehot.T, raw, precision=lax.Precision.HIGHEST)

    layer_ids = jnp.arange(LAYERS).astype(jnp.int32)
    edge_scores = lax.map(score_one, (head_delta, out_proj, node_map, layer_ids))
    return residual_grad, edge_scores
```

```python
import jax
import jax.numpy as jnp
from jax import lax
from jax.sharding import PartitionSpec as P

HEADS = 32
HEAD_DIM = 128
KV = 4
PROMPT = 32
GROUP = 8


def on_device(grad_in, out_proj, value_proj, head_delta, pattern, positions, node_map):
    tokens = grad_in.shape[1]
    local_width = grad_in.shape[2]
    own_rows = out_proj.shape[1]
    own_heads = own_rows // HEAD_DIM
    width = out_proj.shape[2]
    tp_count = lax.axis_size("tp")
    section_count = lax.axis_size("section")
    weights = out_proj[0]

    blocks = weights.reshape(own_rows, tp_count, width // tp_count).transpose(1, 0, 2)
    column_blocks = lax.all_to_all(blocks, "tp", 0, 0, tiled=True)
    all_delta_cols = lax.all_gather(head_delta[0], "tp", axis=1, tiled=True)

    token_ids = jnp.arange(tokens)
    block_ids = token_ids // PROMPT
    allowed = (
        (block_ids[:, None] == block_ids[None, :])
        & (positions[None, :] >= 0)
        & (positions[None, :] <= positions[:, None])
    )
    visible = allowed.astype(jnp.bfloat16)
    grad_rows = lax.all_gather(grad_in[0], "tp", axis=1, tiled=True)
    head_grad = lax.dot_general(
        grad_rows,
        weights,
        (((1,), (1,)), ((), ())),
        preferred_element_type=jnp.float32,
    ).astype(jnp.bfloat16)
    masked = pattern[0] * visible[None]
    value_grad = jnp.einsum(
        "hts,thc->shc",
        masked,
        head_grad.reshape(tokens, own_heads, HEAD_DIM),
        preferred_element_type=jnp.float32,
    ).astype(jnp.bfloat16)
    pair_sum = value_grad.astype(jnp.float32).sum(axis=1)
    group_of = (lax.axis_index("tp") * own_heads) // GROUP
    slots = jnp.zeros((tokens, KV, HEAD_DIM), jnp.float32)
    slots = lax.dynamic_update_slice(slots, pair_sum[:, None, :], (0, group_of, 0))
    summed = lax.psum(slots, "tp")
    group_grad = summed.reshape(tokens, KV * HEAD_DIM).astype(jnp.bfloat16)
    increment = lax.dot_general(
        group_grad, value_proj[0], (((1,), (1,)), ((), ())), preferred_element_type=jnp.float32
    )
    residual_grad = (grad_in[0].astype(jnp.float32) + increment).astype(jnp.bfloat16)
    target_row = increment.astype(jnp.bfloat16)
    target_rows = lax.all_gather(target_row[None], "section", axis=0, tiled=True)

    delta = jnp.einsum(
        "thc,hcd->htd",
        all_delta_cols.reshape(tokens, HEADS, HEAD_DIM),
        column_blocks.reshape(HEADS, HEAD_DIM, local_width),
        preferred_element_type=jnp.float32,
    ).astype(jnp.bfloat16)
    partial_scores = lax.dot_general(
        delta.reshape(HEADS, tokens * local_width),
        target_rows.reshape(section_count, tokens * local_width),
        (((1,), (1,)), ((), ())),
        preferred_element_type=jnp.float32,
    )
    totals = lax.psum(partial_scores, "tp")
    later = jnp.arange(section_count) > lax.axis_index("section")
    raw_scores = jnp.where(later[None, :], totals / tokens, jnp.zeros_like(totals))
    onehot = (node_map[0][:, None] == jnp.arange(HEADS)[None, :]).astype(jnp.float32)
    edge_scores = jnp.dot(onehot.T, raw_scores, precision=lax.Precision.HIGHEST)
    return (residual_grad[None], edge_scores[None])


def solution(mesh):
    placed = (
        P("section", None, "tp"),
        P("section", "tp", None),
        P("section", "tp", None),
        P("section", None, "tp"),
        P("section", "tp", None, None),
        P(),
        P("section", None),
    )
    return jax.shard_map(
        on_device,
        mesh=mesh,
        in_specs=placed,
        out_specs=(P("section", None, "tp"), P("section", None, None)),
        check_vma=False,
    )
```

```python
import jax
import jax.numpy as jnp
import numpy as np
from jax import lax
from jax.sharding import Mesh
from jax.sharding import PartitionSpec as P

HEADS = 32
HEAD_DIM = 128
KV = 4
PROMPT = 32
GROUP = 8
TP = ("zl", "x")


def from_everyone(array, axis):
    count = lax.axis_size(axis)
    return lax.all_to_all(
        jnp.broadcast_to(array[None], (count, *array.shape)), axis, 0, 0, tiled=True
    )


def on_device(grad_in, out_proj, value_proj, head_delta, pattern, positions, node_map):
    tokens = grad_in.shape[1]
    local_width = grad_in.shape[2]
    own_rows = out_proj.shape[1]
    own_heads = own_rows // HEAD_DIM
    width = out_proj.shape[2]
    tp_count = lax.axis_size(TP)
    section_count = lax.axis_size("section")
    weights = out_proj[0]

    own_delta = jnp.einsum(
        "thc,hcd->htd",
        head_delta[0].reshape(tokens, own_heads, HEAD_DIM),
        weights.reshape(own_heads, HEAD_DIM, width),
        preferred_element_type=jnp.float32,
    ).astype(jnp.bfloat16)
    pieces = own_delta.reshape(own_heads, tokens, tp_count, local_width).transpose(2, 0, 1, 3)
    delta = lax.all_to_all(pieces, TP, 0, 0, tiled=True)

    token_ids = jnp.arange(tokens)
    block_ids = token_ids // PROMPT
    allowed = (
        (block_ids[:, None] == block_ids[None, :])
        & (positions[None, :] >= 0)
        & (positions[None, :] <= positions[:, None])
    )
    visible = allowed.astype(jnp.bfloat16)
    everyone = from_everyone(grad_in[0], TP)
    grad_rows = jnp.moveaxis(everyone, 0, 1).reshape(tokens, width)
    head_grad = lax.dot_general(
        grad_rows,
        weights,
        (((1,), (1,)), ((), ())),
        preferred_element_type=jnp.float32,
    ).astype(jnp.bfloat16)
    masked = pattern[0] * visible[None]
    value_grad = jnp.einsum(
        "hts,thc->shc",
        masked,
        head_grad.reshape(tokens, own_heads, HEAD_DIM),
        preferred_element_type=jnp.float32,
    ).astype(jnp.bfloat16)
    pair_sum = value_grad.astype(jnp.float32).sum(axis=1)
    group_sum = from_everyone(pair_sum, "x").sum(axis=0).astype(jnp.bfloat16)
    groups = from_everyone(group_sum, "zl")
    group_grad = jnp.moveaxis(groups, 0, 1).reshape(tokens, KV * HEAD_DIM)
    increment = lax.dot_general(
        group_grad, value_proj[0], (((1,), (1,)), ((), ())), preferred_element_type=jnp.float32
    )
    residual_grad = (grad_in[0].astype(jnp.float32) + increment).astype(jnp.bfloat16)
    target_row = increment.astype(jnp.bfloat16)
    target_rows = lax.all_gather(target_row[None], "section", axis=0, tiled=True)

    partial_scores = lax.dot_general(
        delta.reshape(HEADS, tokens * local_width),
        target_rows.reshape(section_count, tokens * local_width),
        (((1,), (1,)), ((), ())),
        preferred_element_type=jnp.float32,
    )
    row_sum = from_everyone(partial_scores, "x").sum(axis=0)
    totals = from_everyone(row_sum, "zl").sum(axis=0)
    later = jnp.arange(section_count) > lax.axis_index("section")
    raw_scores = jnp.where(later[None, :], totals / tokens, jnp.zeros_like(totals))
    onehot = (node_map[0][:, None] == jnp.arange(HEADS)[None, :]).astype(jnp.float32)
    edge_scores = jnp.dot(onehot.T, raw_scores, precision=lax.Precision.HIGHEST)
    return (residual_grad[None], edge_scores[None])


def solution(mesh):
    sections, tps = mesh.devices.shape
    side = int(round(np.sqrt(tps)))
    fine = Mesh(mesh.devices.reshape(sections, tps // side, side), ("section",) + TP)
    placed = (
        P("section", None, TP),
        P("section", TP, None),
        P("section", TP, None),
        P("section", None, TP),
        P("section", TP, None, None),
        P(),
        P("section", None),
    )
    return jax.shard_map(
        on_device,
        mesh=fine,
        in_specs=placed,
        out_specs=(P("section", None, TP), P("section", None, None)),
        check_vma=False,
    )
```

```python
import jax
import jax.numpy as jnp
import numpy as np
from jax import lax
from jax.sharding import Mesh
from jax.sharding import PartitionSpec as P

HEADS = 32
HEAD_DIM = 128
KV = 4
PROMPT = 32
GROUP = 8
TP = ("zl", "x")
SECTION = ("zh", "y", "core")
PLANE = ("zh", "y")


def from_everyone(array, axis):
    count = lax.axis_size(axis)
    return lax.all_to_all(
        jnp.broadcast_to(array[None], (count, *array.shape)), axis, 0, 0, tiled=True
    )


def on_device(grad_in, out_proj, value_proj, head_delta, pattern, positions, node_map):
    tokens = grad_in.shape[1]
    local_width = grad_in.shape[2]
    own_rows = out_proj.shape[1]
    own_heads = own_rows // HEAD_DIM
    width = out_proj.shape[2]
    tp_count = lax.axis_size(TP)
    section_count = lax.axis_size(SECTION)
    weights = out_proj[0]

    own_delta = jnp.einsum(
        "thc,hcd->htd",
        head_delta[0].reshape(tokens, own_heads, HEAD_DIM),
        weights.reshape(own_heads, HEAD_DIM, width),
        preferred_element_type=jnp.float32,
    ).astype(jnp.bfloat16)
    pieces = own_delta.reshape(own_heads, tokens, tp_count, local_width).transpose(2, 0, 1, 3)
    delta = lax.all_to_all(pieces, TP, 0, 0, tiled=True)

    token_ids = jnp.arange(tokens)
    block_ids = token_ids // PROMPT
    allowed = (
        (block_ids[:, None] == block_ids[None, :])
        & (positions[None, :] >= 0)
        & (positions[None, :] <= positions[:, None])
    )
    visible = allowed.astype(jnp.bfloat16)
    everyone = from_everyone(grad_in[0], TP)
    grad_rows = jnp.moveaxis(everyone, 0, 1).reshape(tokens, width)
    head_grad = lax.dot_general(
        grad_rows,
        weights,
        (((1,), (1,)), ((), ())),
        preferred_element_type=jnp.float32,
    ).astype(jnp.bfloat16)
    masked = pattern[0] * visible[None]
    value_grad = jnp.einsum(
        "hts,thc->shc",
        masked,
        head_grad.reshape(tokens, own_heads, HEAD_DIM),
        preferred_element_type=jnp.float32,
    ).astype(jnp.bfloat16)
    pair_sum = value_grad.astype(jnp.float32).sum(axis=1)
    group_sum = from_everyone(pair_sum, "x").sum(axis=0).astype(jnp.bfloat16)
    groups = from_everyone(group_sum, "zl")
    group_grad = jnp.moveaxis(groups, 0, 1).reshape(tokens, KV * HEAD_DIM)
    increment = lax.dot_general(
        group_grad, value_proj[0], (((1,), (1,)), ((), ())), preferred_element_type=jnp.float32
    )
    residual_grad = (grad_in[0].astype(jnp.float32) + increment).astype(jnp.bfloat16)
    target_row = increment.astype(jnp.bfloat16)
    mine = lax.all_gather(target_row, PLANE, axis=0, tiled=False)
    core = lax.axis_index("core")
    theirs = lax.ppermute(mine, "core", [(0, 1), (1, 0)])
    all_heads = delta.reshape(HEADS, tokens, local_width)
    contract = (((1, 2), (1, 2)), ((), ()))
    with_mine = lax.dot_general(all_heads, mine, contract, preferred_element_type=jnp.float32)
    with_theirs = lax.dot_general(all_heads, theirs, contract, preferred_element_type=jnp.float32)
    first = jnp.where(core == 0, with_mine, with_theirs)
    second = jnp.where(core == 0, with_theirs, with_mine)
    partial_scores = jnp.stack([first, second], axis=-1).reshape(HEADS, section_count)
    totals = from_everyone(partial_scores, TP).sum(axis=0)
    later = jnp.arange(section_count) > lax.axis_index(SECTION)
    raw_scores = jnp.where(later[None, :], totals / tokens, jnp.zeros_like(totals))
    onehot = (node_map[0][:, None] == jnp.arange(HEADS)[None, :]).astype(jnp.float32)
    edge_scores = jnp.dot(onehot.T, raw_scores, precision=lax.Precision.HIGHEST)
    return (residual_grad[None], edge_scores[None])


def solution(mesh):
    sections, tps = mesh.devices.shape
    side = int(round(np.sqrt(tps)))
    cores = 2
    rows = int(round(np.sqrt(sections // cores)))
    fine = Mesh(
        mesh.devices.reshape(sections // cores // rows, rows, cores, tps // side, side),
        SECTION + TP,
    )
    placed = (
        P(SECTION, None, TP),
        P(SECTION, TP, None),
        P(SECTION, TP, None),
        P(SECTION, None, TP),
        P(SECTION, TP, None, None),
        P(),
        P(SECTION, None),
    )
    return jax.shard_map(
        on_device,
        mesh=fine,
        in_specs=placed,
        out_specs=(P(SECTION, None, TP), P(SECTION, None, None)),
        check_vma=False,
    )
```

```python
import jax
import jax.numpy as jnp
import numpy as np
from jax import lax
from jax.sharding import Mesh
from jax.sharding import PartitionSpec as P

HEADS = 32
HEAD_DIM = 128
KV = 4
PROMPT = 32
GROUP = 8
TP = ("zl", "x")
SECTION = ("zh", "y", "core")
PLANE = ("zh", "y")


def from_everyone(array, axis):
    count = lax.axis_size(axis)
    return lax.all_to_all(
        jnp.broadcast_to(array[None], (count, *array.shape)), axis, 0, 0, tiled=True
    )


def gathered(piece):
    column = from_everyone(piece, "zl")
    row = from_everyone(column, "x")
    tokens = piece.shape[0]
    return jnp.transpose(row, (2, 1, 0, 3)).reshape(tokens, -1)


def on_device(grad_in, out_proj, value_proj, head_delta, pattern, positions, node_map):
    tokens = grad_in.shape[1]
    local_width = grad_in.shape[2]
    own_rows = out_proj.shape[1]
    own_heads = own_rows // HEAD_DIM
    width = out_proj.shape[2]
    tp_count = lax.axis_size(TP)
    section_count = lax.axis_size(SECTION)
    weights = out_proj[0]

    blocks = weights.reshape(own_rows, tp_count, local_width).transpose(1, 0, 2)
    column_blocks = lax.all_to_all(blocks, TP, 0, 0, tiled=True)
    delta_cols = gathered(head_delta[0])

    token_ids = jnp.arange(tokens)
    block_ids = token_ids // PROMPT
    allowed = (
        (block_ids[:, None] == block_ids[None, :])
        & (positions[None, :] >= 0)
        & (positions[None, :] <= positions[:, None])
    )
    visible = allowed.astype(jnp.bfloat16)
    grad_rows = gathered(grad_in[0])
    head_grad = lax.dot_general(
        grad_rows,
        weights,
        (((1,), (1,)), ((), ())),
        preferred_element_type=jnp.float32,
    ).astype(jnp.bfloat16)
    masked = pattern[0] * visible[None]
    value_grad = jnp.einsum(
        "hts,thc->shc",
        masked,
        head_grad.reshape(tokens, own_heads, HEAD_DIM),
        preferred_element_type=jnp.float32,
    ).astype(jnp.bfloat16)
    pair_sum = value_grad.astype(jnp.float32).sum(axis=1)
    group_sum = from_everyone(pair_sum, "x").sum(axis=0).astype(jnp.bfloat16)
    groups = from_everyone(group_sum, "zl")
    group_grad = jnp.moveaxis(groups, 0, 1).reshape(tokens, KV * HEAD_DIM)
    increment = lax.dot_general(
        group_grad, value_proj[0], (((1,), (1,)), ((), ())), preferred_element_type=jnp.float32
    )
    residual_grad = (grad_in[0].astype(jnp.float32) + increment).astype(jnp.bfloat16)
    target_row = increment.astype(jnp.bfloat16)
    mine = lax.all_gather(target_row, PLANE, axis=0, tiled=False)
    core = lax.axis_index("core")
    theirs = lax.ppermute(mine, "core", [(0, 1), (1, 0)])
    all_heads = jnp.einsum(
        "thc,hcd->htd",
        delta_cols.reshape(tokens, HEADS, HEAD_DIM),
        column_blocks.reshape(HEADS, HEAD_DIM, local_width),
        preferred_element_type=jnp.float32,
    ).astype(jnp.bfloat16)
    contract = (((1, 2), (1, 2)), ((), ()))
    with_mine = lax.dot_general(all_heads, mine, contract, preferred_element_type=jnp.float32)
    with_theirs = lax.dot_general(all_heads, theirs, contract, preferred_element_type=jnp.float32)
    first = jnp.where(core == 0, with_mine, with_theirs)
    second = jnp.where(core == 0, with_theirs, with_mine)
    partial_scores = jnp.stack([first, second], axis=-1).reshape(HEADS, section_count)
    totals = from_everyone(partial_scores, TP).sum(axis=0)
    later = jnp.arange(section_count) > lax.axis_index(SECTION)
    raw_scores = jnp.where(later[None, :], totals / tokens, jnp.zeros_like(totals))
    onehot = (node_map[0][:, None] == jnp.arange(HEADS)[None, :]).astype(jnp.float32)
    edge_scores = jnp.dot(onehot.T, raw_scores, precision=lax.Precision.HIGHEST)
    return (residual_grad[None], edge_scores[None])


def solution(mesh):
    sections, tps = mesh.devices.shape
    side = int(round(np.sqrt(tps)))
    cores = 2
    rows = int(round(np.sqrt(sections // cores)))
    fine = Mesh(
        mesh.devices.reshape(sections // cores // rows, rows, cores, tps // side, side),
        SECTION + TP,
    )
    placed = (
        P(SECTION, None, TP),
        P(SECTION, TP, None),
        P(SECTION, TP, None),
        P(SECTION, None, TP),
        P(SECTION, TP, None, None),
        P(),
        P(SECTION, None),
    )
    return jax.shard_map(
        on_device,
        mesh=fine,
        in_specs=placed,
        out_specs=(P(SECTION, None, TP), P(SECTION, None, None)),
        check_vma=False,
    )
```

```python
import jax
import jax.numpy as jnp
import numpy as np
from jax import lax
from jax.sharding import Mesh
from jax.sharding import PartitionSpec as P

HEADS = 32
HEAD_DIM = 128
KV = 4
PROMPT = 32
GROUP = 8
TP = ("zl", "x")
SECTION = ("zh", "y", "core")
PLANE = ("zh", "y")


def from_everyone(array, axis):
    count = lax.axis_size(axis)
    return lax.all_to_all(
        jnp.broadcast_to(array[None], (count, *array.shape)), axis, 0, 0, tiled=True
    )


def by_permutes(array, axis):
    count = lax.axis_size(axis)
    me = lax.axis_index(axis)
    shifted = [array] + [
        lax.ppermute(array, axis, [(i, (i + k) % count) for i in range(count)])
        for k in range(1, count)
    ]
    stacked = jnp.stack(shifted)
    return jnp.take(stacked, (me - jnp.arange(count)) % count, axis=0)


def gathered(piece):
    column = by_permutes(piece, "zl")
    row = by_permutes(column, "x")
    tokens = piece.shape[0]
    return jnp.transpose(row, (2, 1, 0, 3)).reshape(tokens, -1)


def on_device(grad_in, out_proj, value_proj, head_delta, pattern, positions, node_map):
    tokens = grad_in.shape[1]
    local_width = grad_in.shape[2]
    own_rows = out_proj.shape[1]
    own_heads = own_rows // HEAD_DIM
    width = out_proj.shape[2]
    tp_count = lax.axis_size(TP)
    section_count = lax.axis_size(SECTION)
    weights = out_proj[0]

    own_delta = jnp.einsum(
        "thc,hcd->htd",
        head_delta[0].reshape(tokens, own_heads, HEAD_DIM),
        weights.reshape(own_heads, HEAD_DIM, width),
        preferred_element_type=jnp.float32,
    ).astype(jnp.bfloat16)
    pieces = own_delta.reshape(own_heads, tokens, tp_count, local_width).transpose(2, 0, 1, 3)
    delta = lax.all_to_all(pieces, TP, 0, 0, tiled=True)

    token_ids = jnp.arange(tokens)
    block_ids = token_ids // PROMPT
    allowed = (
        (block_ids[:, None] == block_ids[None, :])
        & (positions[None, :] >= 0)
        & (positions[None, :] <= positions[:, None])
    )
    visible = allowed.astype(jnp.bfloat16)
    grad_rows = gathered(grad_in[0])
    head_grad = lax.dot_general(
        grad_rows,
        weights,
        (((1,), (1,)), ((), ())),
        preferred_element_type=jnp.float32,
    ).astype(jnp.bfloat16)
    masked = pattern[0] * visible[None]
    value_grad = jnp.einsum(
        "hts,thc->shc",
        masked,
        head_grad.reshape(tokens, own_heads, HEAD_DIM),
        preferred_element_type=jnp.float32,
    ).astype(jnp.bfloat16)
    pair_sum = value_grad.astype(jnp.float32).sum(axis=1)
    group_sum = by_permutes(pair_sum, "x").sum(axis=0).astype(jnp.bfloat16)
    groups = by_permutes(group_sum, "zl")
    group_grad = jnp.moveaxis(groups, 0, 1).reshape(tokens, KV * HEAD_DIM)
    increment = lax.dot_general(
        group_grad, value_proj[0], (((1,), (1,)), ((), ())), preferred_element_type=jnp.float32
    )
    residual_grad = (grad_in[0].astype(jnp.float32) + increment).astype(jnp.bfloat16)
    target_row = increment.astype(jnp.bfloat16)
    mine = lax.all_gather(target_row, PLANE, axis=0, tiled=False)
    core = lax.axis_index("core")
    theirs = lax.ppermute(mine, "core", [(0, 1), (1, 0)])
    all_heads = delta.reshape(HEADS, tokens, local_width)
    contract = (((1, 2), (1, 2)), ((), ()))
    with_mine = lax.dot_general(all_heads, mine, contract, preferred_element_type=jnp.float32)
    with_theirs = lax.dot_general(all_heads, theirs, contract, preferred_element_type=jnp.float32)
    first = jnp.where(core == 0, with_mine, with_theirs)
    second = jnp.where(core == 0, with_theirs, with_mine)
    partial_scores = jnp.stack([first, second], axis=-1).reshape(HEADS, section_count)
    totals = from_everyone(partial_scores, TP).sum(axis=0)
    later = jnp.arange(section_count) > lax.axis_index(SECTION)
    raw_scores = jnp.where(later[None, :], totals / tokens, jnp.zeros_like(totals))
    onehot = (node_map[0][:, None] == jnp.arange(HEADS)[None, :]).astype(jnp.float32)
    edge_scores = jnp.dot(onehot.T, raw_scores, precision=lax.Precision.HIGHEST)
    return (residual_grad[None], edge_scores[None])


def solution(mesh):
    sections, tps = mesh.devices.shape
    side = int(round(np.sqrt(tps)))
    cores = 2
    rows = int(round(np.sqrt(sections // cores)))
    fine = Mesh(
        mesh.devices.reshape(sections // cores // rows, rows, cores, tps // side, side),
        SECTION + TP,
    )
    placed = (
        P(SECTION, None, TP),
        P(SECTION, TP, None),
        P(SECTION, TP, None),
        P(SECTION, None, TP),
        P(SECTION, TP, None, None),
        P(),
        P(SECTION, None),
    )
    return jax.shard_map(
        on_device,
        mesh=fine,
        in_specs=placed,
        out_specs=(P(SECTION, None, TP), P(SECTION, None, None)),
        check_vma=False,
    )
```

```python
import jax
import jax.numpy as jnp
import numpy as np
from jax import lax
from jax.sharding import Mesh
from jax.sharding import PartitionSpec as P

HEADS = 32
HEAD_DIM = 128
KV = 4
PROMPT = 32
GROUP = 8
TP = ("zl", "x")
SECTION = ("zh", "y", "core")
PLANE = ("zh", "y")


def from_everyone(array, axis):
    count = lax.axis_size(axis)
    return lax.all_to_all(
        jnp.broadcast_to(array[None], (count, *array.shape)), axis, 0, 0, tiled=True
    )


def on_device(grad_in, out_proj, value_proj, head_delta, pattern, positions, node_map):
    tokens = grad_in.shape[1]
    local_width = grad_in.shape[2]
    own_rows = out_proj.shape[1]
    own_heads = own_rows // HEAD_DIM
    width = out_proj.shape[2]
    tp_count = lax.axis_size(TP)
    section_count = lax.axis_size(SECTION)
    weights = out_proj[0]

    own_delta = jnp.einsum(
        "thc,hcd->htd",
        head_delta[0].reshape(tokens, own_heads, HEAD_DIM),
        weights.reshape(own_heads, HEAD_DIM, width),
        preferred_element_type=jnp.float32,
    ).astype(jnp.bfloat16)
    pieces = own_delta.reshape(own_heads, tokens, tp_count, local_width).transpose(2, 0, 1, 3)
    delta = lax.all_to_all(pieces, TP, 0, 0, tiled=True)

    token_ids = jnp.arange(tokens)
    block_ids = token_ids // PROMPT
    allowed = (
        (block_ids[:, None] == block_ids[None, :])
        & (positions[None, :] >= 0)
        & (positions[None, :] <= positions[:, None])
    )
    visible = allowed.astype(jnp.bfloat16)
    everyone = from_everyone(grad_in[0], TP)
    grad_rows = jnp.moveaxis(everyone, 0, 1).reshape(tokens, width)
    head_grad = lax.dot_general(
        grad_rows,
        weights,
        (((1,), (1,)), ((), ())),
        preferred_element_type=jnp.float32,
    ).astype(jnp.bfloat16)
    masked = pattern[0] * visible[None]
    value_grad = jnp.einsum(
        "hts,thc->shc",
        masked,
        head_grad.reshape(tokens, own_heads, HEAD_DIM),
        preferred_element_type=jnp.float32,
    ).astype(jnp.bfloat16)
    pair_sum = value_grad.astype(jnp.float32).sum(axis=1)
    group_sum = from_everyone(pair_sum, "x").sum(axis=0).astype(jnp.bfloat16)
    groups = from_everyone(group_sum, "zl")
    group_grad = jnp.moveaxis(groups, 0, 1).reshape(tokens, KV * HEAD_DIM)
    increment = lax.dot_general(
        group_grad, value_proj[0], (((1,), (1,)), ((), ())), preferred_element_type=jnp.float32
    )
    residual_grad = (grad_in[0].astype(jnp.float32) + increment).astype(jnp.bfloat16)
    target_row = increment.astype(jnp.bfloat16)
    mine = lax.all_gather(target_row, PLANE, axis=0, tiled=False)
    core = lax.axis_index("core")
    theirs = lax.ppermute(mine, "core", [(0, 1), (1, 0)])
    all_heads = delta.reshape(HEADS, tokens, local_width)
    contract = (((1, 2), (1, 2)), ((), ()))
    both = jnp.concatenate([mine, theirs], axis=0)
    scores = lax.dot_general(all_heads, both, contract, preferred_element_type=jnp.float32)
    half = scores.shape[1] // 2
    first = jnp.where(core == 0, scores[:, :half], scores[:, half:])
    second = jnp.where(core == 0, scores[:, half:], scores[:, :half])
    partial_scores = jnp.stack([first, second], axis=-1).reshape(HEADS, section_count)
    totals = from_everyone(partial_scores, TP).sum(axis=0)
    later = jnp.arange(section_count) > lax.axis_index(SECTION)
    raw_scores = jnp.where(later[None, :], totals / tokens, jnp.zeros_like(totals))
    onehot = (node_map[0][:, None] == jnp.arange(HEADS)[None, :]).astype(jnp.float32)
    edge_scores = jnp.dot(onehot.T, raw_scores, precision=lax.Precision.HIGHEST)
    return (residual_grad[None], edge_scores[None])


def solution(mesh):
    sections, tps = mesh.devices.shape
    side = int(round(np.sqrt(tps)))
    cores = 2
    rows = int(round(np.sqrt(sections // cores)))
    fine = Mesh(
        mesh.devices.reshape(sections // cores // rows, rows, cores, tps // side, side),
        SECTION + TP,
    )
    placed = (
        P(SECTION, None, TP),
        P(SECTION, TP, None),
        P(SECTION, TP, None),
        P(SECTION, None, TP),
        P(SECTION, TP, None, None),
        P(),
        P(SECTION, None),
    )
    return jax.shard_map(
        on_device,
        mesh=fine,
        in_specs=placed,
        out_specs=(P(SECTION, None, TP), P(SECTION, None, None)),
        check_vma=False,
    )
```

```python
import jax
import jax.numpy as jnp
import numpy as np
from jax import lax
from jax.sharding import Mesh
from jax.sharding import PartitionSpec as P

HEADS = 32
HEAD_DIM = 128
KV = 4
PROMPT = 32
GROUP = 8
TP = ("zl", "x")
SECTION = ("zh", "y", "core")
PLANE = ("zh", "y")


def from_everyone(array, axis):
    count = lax.axis_size(axis)
    return lax.all_to_all(
        jnp.broadcast_to(array[None], (count, *array.shape)), axis, 0, 0, tiled=True
    )


def gathered(piece):
    column = from_everyone(piece, "zl")
    row = from_everyone(column, "x")
    tokens = piece.shape[0]
    return jnp.transpose(row, (2, 1, 0, 3)).reshape(tokens, -1)


def on_device(grad_in, out_proj, value_proj, head_delta, pattern, positions, node_map):
    tokens = grad_in.shape[1]
    local_width = grad_in.shape[2]
    own_rows = out_proj.shape[1]
    own_heads = own_rows // HEAD_DIM
    width = out_proj.shape[2]
    tp_count = lax.axis_size(TP)
    section_count = lax.axis_size(SECTION)
    weights = out_proj[0]

    blocks = weights.reshape(own_rows, tp_count, local_width).transpose(1, 0, 2)
    column_blocks = lax.all_to_all(blocks, TP, 0, 0, tiled=True)

    token_ids = jnp.arange(tokens)
    block_ids = token_ids // PROMPT
    allowed = (
        (block_ids[:, None] == block_ids[None, :])
        & (positions[None, :] >= 0)
        & (positions[None, :] <= positions[:, None])
    )
    visible = allowed.astype(jnp.bfloat16)
    everyone = from_everyone(grad_in[0], TP)
    grad_rows = jnp.moveaxis(everyone, 0, 1).reshape(tokens, width)
    head_grad = lax.dot_general(
        grad_rows,
        weights,
        (((1,), (1,)), ((), ())),
        preferred_element_type=jnp.float32,
    ).astype(jnp.bfloat16)
    masked = pattern[0] * visible[None]
    value_grad = jnp.einsum(
        "hts,thc->shc",
        masked,
        head_grad.reshape(tokens, own_heads, HEAD_DIM),
        preferred_element_type=jnp.float32,
    ).astype(jnp.bfloat16)
    pair_sum = value_grad.astype(jnp.float32).sum(axis=1)
    group_sum = from_everyone(pair_sum, "x").sum(axis=0).astype(jnp.bfloat16)
    groups = from_everyone(group_sum, "zl")
    group_grad = jnp.moveaxis(groups, 0, 1).reshape(tokens, KV * HEAD_DIM)
    increment = lax.dot_general(
        group_grad, value_proj[0], (((1,), (1,)), ((), ())), preferred_element_type=jnp.float32
    )
    residual_grad = (grad_in[0].astype(jnp.float32) + increment).astype(jnp.bfloat16)
    target_row = increment.astype(jnp.bfloat16)
    mine = lax.all_gather(target_row, PLANE, axis=0, tiled=False)
    delta_piece, target_row = lax.optimization_barrier((head_delta[0], target_row))
    delta_cols = gathered(delta_piece)
    core = lax.axis_index("core")
    theirs = lax.ppermute(mine, "core", [(0, 1), (1, 0)])
    all_heads = jnp.einsum(
        "thc,hcd->htd",
        delta_cols.reshape(tokens, HEADS, HEAD_DIM),
        column_blocks.reshape(HEADS, HEAD_DIM, local_width),
        preferred_element_type=jnp.float32,
    ).astype(jnp.bfloat16)
    contract = (((1, 2), (1, 2)), ((), ()))
    both = jnp.concatenate([mine, theirs], axis=0)
    scores = lax.dot_general(all_heads, both, contract, preferred_element_type=jnp.float32)
    half = scores.shape[1] // 2
    first = jnp.where(core == 0, scores[:, :half], scores[:, half:])
    second = jnp.where(core == 0, scores[:, half:], scores[:, :half])
    partial_scores = jnp.stack([first, second], axis=-1).reshape(HEADS, section_count)
    totals = from_everyone(partial_scores, TP).sum(axis=0)
    later = jnp.arange(section_count) > lax.axis_index(SECTION)
    raw_scores = jnp.where(later[None, :], totals / tokens, jnp.zeros_like(totals))
    onehot = (node_map[0][:, None] == jnp.arange(HEADS)[None, :]).astype(jnp.float32)
    edge_scores = jnp.dot(onehot.T, raw_scores, precision=lax.Precision.HIGHEST)
    return (residual_grad[None], edge_scores[None])


def solution(mesh):
    sections, tps = mesh.devices.shape
    side = int(round(np.sqrt(tps)))
    cores = 2
    rows = int(round(np.sqrt(sections // cores)))
    fine = Mesh(
        mesh.devices.reshape(sections // cores // rows, rows, cores, tps // side, side),
        SECTION + TP,
    )
    placed = (
        P(SECTION, None, TP),
        P(SECTION, TP, None),
        P(SECTION, TP, None),
        P(SECTION, None, TP),
        P(SECTION, TP, None, None),
        P(),
        P(SECTION, None),
    )
    return jax.shard_map(
        on_device,
        mesh=fine,
        in_specs=placed,
        out_specs=(P(SECTION, None, TP), P(SECTION, None, None)),
        check_vma=False,
    )
```

```python
import jax
import jax.numpy as jnp
import numpy as np
from jax import lax
from jax.sharding import Mesh
from jax.sharding import PartitionSpec as P

HEADS = 32
HEAD_DIM = 128
KV = 4
PROMPT = 32
GROUP = 8
TP = ("zl", "x")
SECTION = ("zh", "y", "core")


def from_everyone(array, axis):
    count = lax.axis_size(axis)
    return lax.all_to_all(
        jnp.broadcast_to(array[None], (count, *array.shape)), axis, 0, 0, tiled=True
    )


def on_device(grad_in, out_proj, value_proj, head_delta, pattern, positions, node_map):
    tokens = grad_in.shape[1]
    local_width = grad_in.shape[2]
    own_rows = out_proj.shape[1]
    own_heads = own_rows // HEAD_DIM
    width = out_proj.shape[2]
    tp_count = lax.axis_size(TP)
    section_count = lax.axis_size(SECTION)
    weights = out_proj[0]

    own_delta = jnp.einsum(
        "thc,hcd->htd",
        head_delta[0].reshape(tokens, own_heads, HEAD_DIM),
        weights.reshape(own_heads, HEAD_DIM, width),
        preferred_element_type=jnp.float32,
    ).astype(jnp.bfloat16)
    pieces = own_delta.reshape(own_heads, tokens, tp_count, local_width).transpose(2, 0, 1, 3)
    delta = lax.all_to_all(pieces, TP, 0, 0, tiled=True)

    token_ids = jnp.arange(tokens)
    block_ids = token_ids // PROMPT
    allowed = (
        (block_ids[:, None] == block_ids[None, :])
        & (positions[None, :] >= 0)
        & (positions[None, :] <= positions[:, None])
    )
    visible = allowed.astype(jnp.bfloat16)
    everyone = from_everyone(grad_in[0], TP)
    grad_rows = jnp.moveaxis(everyone, 0, 1).reshape(tokens, width)
    head_grad = lax.dot_general(
        grad_rows,
        weights,
        (((1,), (1,)), ((), ())),
        preferred_element_type=jnp.float32,
    ).astype(jnp.bfloat16)
    masked = pattern[0] * visible[None]
    value_grad = jnp.einsum(
        "hts,thc->shc",
        masked,
        head_grad.reshape(tokens, own_heads, HEAD_DIM),
        preferred_element_type=jnp.float32,
    ).astype(jnp.bfloat16)
    pair_sum = value_grad.astype(jnp.float32).sum(axis=1)
    group_sum = from_everyone(pair_sum, "x").sum(axis=0).astype(jnp.bfloat16)
    groups = from_everyone(group_sum, "zl")
    group_grad = jnp.moveaxis(groups, 0, 1).reshape(tokens, KV * HEAD_DIM)
    increment = lax.dot_general(
        group_grad, value_proj[0], (((1,), (1,)), ((), ())), preferred_element_type=jnp.float32
    )
    residual_grad = (grad_in[0].astype(jnp.float32) + increment).astype(jnp.bfloat16)
    target_row = increment.astype(jnp.bfloat16)
    target_rows = lax.all_gather(target_row, SECTION, axis=0, tiled=False)
    all_heads = delta.reshape(HEADS, tokens, local_width)
    contract = (((1, 2), (1, 2)), ((), ()))
    partial_scores = lax.dot_general(
        all_heads, target_rows, contract, preferred_element_type=jnp.float32
    )
    totals = from_everyone(partial_scores, TP).sum(axis=0)
    later = jnp.arange(section_count) > lax.axis_index(SECTION)
    raw_scores = jnp.where(later[None, :], totals / tokens, jnp.zeros_like(totals))
    onehot = (node_map[0][:, None] == jnp.arange(HEADS)[None, :]).astype(jnp.float32)
    edge_scores = jnp.dot(onehot.T, raw_scores, precision=lax.Precision.HIGHEST)
    return (residual_grad[None], edge_scores[None])


def solution(mesh):
    sections, tps = mesh.devices.shape
    side = int(round(np.sqrt(tps)))
    cores = 2
    rows = int(round(np.sqrt(sections // cores)))
    fine = Mesh(
        mesh.devices.reshape(sections // cores // rows, rows, cores, tps // side, side),
        SECTION + TP,
    )
    placed = (
        P(SECTION, None, TP),
        P(SECTION, TP, None),
        P(SECTION, TP, None),
        P(SECTION, None, TP),
        P(SECTION, TP, None, None),
        P(),
        P(SECTION, None),
    )
    return jax.shard_map(
        on_device,
        mesh=fine,
        in_specs=placed,
        out_specs=(P(SECTION, None, TP), P(SECTION, None, None)),
        check_vma=False,
    )
```

```python
import jax
import jax.numpy as jnp
import numpy as np
from jax import lax
from jax.sharding import Mesh
from jax.sharding import PartitionSpec as P

HEADS = 32
HEAD_DIM = 128
KV = 4
PROMPT = 32
GROUP = 8
TP = ("zl", "x")
SECTION = ("zh", "y", "core")
PLANE = ("zh", "y")


def from_everyone(array, axis):
    count = lax.axis_size(axis)
    return lax.all_to_all(
        jnp.broadcast_to(array[None], (count, *array.shape)), axis, 0, 0, tiled=True
    )


def gathered(piece):
    column = from_everyone(piece, "zl")
    row = from_everyone(column, "x")
    tokens = piece.shape[0]
    return jnp.transpose(row, (2, 1, 0, 3)).reshape(tokens, -1)


def on_device(grad_in, out_proj, value_proj, head_delta, pattern, positions, node_map):
    tokens = grad_in.shape[1]
    local_width = grad_in.shape[2]
    own_rows = out_proj.shape[1]
    own_heads = own_rows // HEAD_DIM
    width = out_proj.shape[2]
    tp_count = lax.axis_size(TP)
    section_count = lax.axis_size(SECTION)
    weights = out_proj[0]

    blocks = weights.reshape(own_rows, tp_count, local_width).transpose(1, 0, 2)
    column_blocks = lax.all_to_all(blocks, TP, 0, 0, tiled=True)

    token_ids = jnp.arange(tokens)
    block_ids = token_ids // PROMPT
    allowed = (
        (block_ids[:, None] == block_ids[None, :])
        & (positions[None, :] >= 0)
        & (positions[None, :] <= positions[:, None])
    )
    visible = allowed.astype(jnp.bfloat16)
    everyone = from_everyone(grad_in[0], TP)
    grad_rows = jnp.moveaxis(everyone, 0, 1).reshape(tokens, width)
    head_grad = lax.dot_general(
        grad_rows,
        weights,
        (((1,), (1,)), ((), ())),
        preferred_element_type=jnp.float32,
    ).astype(jnp.bfloat16)
    masked = pattern[0] * visible[None]
    value_grad = jnp.einsum(
        "hts,thc->shc",
        masked,
        head_grad.reshape(tokens, own_heads, HEAD_DIM),
        preferred_element_type=jnp.float32,
    ).astype(jnp.bfloat16)
    pair_sum = value_grad.astype(jnp.float32).sum(axis=1)
    group_sum = from_everyone(pair_sum, "x").sum(axis=0).astype(jnp.bfloat16)
    groups = from_everyone(group_sum, "zl")
    group_grad = jnp.moveaxis(groups, 0, 1).reshape(tokens, KV * HEAD_DIM)
    increment = lax.dot_general(
        group_grad, value_proj[0], (((1,), (1,)), ((), ())), preferred_element_type=jnp.float32
    )
    residual_grad = (grad_in[0].astype(jnp.float32) + increment).astype(jnp.bfloat16)
    target_row = increment.astype(jnp.bfloat16)
    mine = lax.all_gather(target_row, PLANE, axis=0, tiled=False)
    delta_piece, column_blocks = lax.optimization_barrier((head_delta[0], column_blocks))
    delta_cols = gathered(delta_piece)
    core = lax.axis_index("core")
    theirs = lax.ppermute(mine, "core", [(0, 1), (1, 0)])
    all_heads = jnp.einsum(
        "thc,hcd->htd",
        delta_cols.reshape(tokens, HEADS, HEAD_DIM),
        column_blocks.reshape(HEADS, HEAD_DIM, local_width),
        preferred_element_type=jnp.float32,
    ).astype(jnp.bfloat16)
    contract = (((1, 2), (1, 2)), ((), ()))
    both = jnp.concatenate([mine, theirs], axis=0)
    scores = lax.dot_general(all_heads, both, contract, preferred_element_type=jnp.float32)
    half = scores.shape[1] // 2
    first = jnp.where(core == 0, scores[:, :half], scores[:, half:])
    second = jnp.where(core == 0, scores[:, half:], scores[:, :half])
    partial_scores = jnp.stack([first, second], axis=-1).reshape(HEADS, section_count)
    totals = from_everyone(partial_scores, TP).sum(axis=0)
    later = jnp.arange(section_count) > lax.axis_index(SECTION)
    raw_scores = jnp.where(later[None, :], totals / tokens, jnp.zeros_like(totals))
    onehot = (node_map[0][:, None] == jnp.arange(HEADS)[None, :]).astype(jnp.float32)
    edge_scores = jnp.dot(onehot.T, raw_scores, precision=lax.Precision.HIGHEST)
    return (residual_grad[None], edge_scores[None])


def solution(mesh):
    sections, tps = mesh.devices.shape
    side = int(round(np.sqrt(tps)))
    cores = 2
    rows = int(round(np.sqrt(sections // cores)))
    fine = Mesh(
        mesh.devices.reshape(sections // cores // rows, rows, cores, tps // side, side),
        SECTION + TP,
    )
    placed = (
        P(SECTION, None, TP),
        P(SECTION, TP, None),
        P(SECTION, TP, None),
        P(SECTION, None, TP),
        P(SECTION, TP, None, None),
        P(),
        P(SECTION, None),
    )
    return jax.shard_map(
        on_device,
        mesh=fine,
        in_specs=placed,
        out_specs=(P(SECTION, None, TP), P(SECTION, None, None)),
        check_vma=False,
    )
```

```python
import jax
import jax.numpy as jnp
import numpy as np
from jax import lax
from jax.sharding import Mesh
from jax.sharding import PartitionSpec as P

HEADS = 32
HEAD_DIM = 128
KV = 4
PROMPT = 32
GROUP = 8
TP = ("zl", "x")
SECTION = ("zh", "y", "core")
PLANE = ("zh", "y")


def from_everyone(array, axis):
    count = lax.axis_size(axis)
    return lax.all_to_all(
        jnp.broadcast_to(array[None], (count, *array.shape)), axis, 0, 0, tiled=True
    )


def on_device(grad_in, out_proj, value_proj, head_delta, pattern, positions, node_map):
    tokens = grad_in.shape[1]
    local_width = grad_in.shape[2]
    own_rows = out_proj.shape[1]
    own_heads = own_rows // HEAD_DIM
    width = out_proj.shape[2]
    tp_count = lax.axis_size(TP)
    section_count = lax.axis_size(SECTION)
    weights = out_proj[0]

    own_delta = jnp.einsum(
        "thc,hcd->htd",
        head_delta[0].reshape(tokens, own_heads, HEAD_DIM),
        weights.reshape(own_heads, HEAD_DIM, width),
        preferred_element_type=jnp.float32,
    ).astype(jnp.bfloat16)
    pieces = own_delta.reshape(own_heads, tokens, tp_count, local_width).transpose(2, 0, 1, 3)

    token_ids = jnp.arange(tokens)
    block_ids = token_ids // PROMPT
    allowed = (
        (block_ids[:, None] == block_ids[None, :])
        & (positions[None, :] >= 0)
        & (positions[None, :] <= positions[:, None])
    )
    visible = allowed.astype(jnp.bfloat16)
    everyone = from_everyone(grad_in[0], TP)
    pieces, everyone = lax.optimization_barrier((pieces, everyone))
    grad_rows = jnp.moveaxis(everyone, 0, 1).reshape(tokens, width)
    head_grad = lax.dot_general(
        grad_rows,
        weights,
        (((1,), (1,)), ((), ())),
        preferred_element_type=jnp.float32,
    ).astype(jnp.bfloat16)
    masked = pattern[0] * visible[None]
    value_grad = jnp.einsum(
        "hts,thc->shc",
        masked,
        head_grad.reshape(tokens, own_heads, HEAD_DIM),
        preferred_element_type=jnp.float32,
    ).astype(jnp.bfloat16)
    pair_sum = value_grad.astype(jnp.float32).sum(axis=1)
    group_sum = from_everyone(pair_sum, "x").sum(axis=0).astype(jnp.bfloat16)
    groups = from_everyone(group_sum, "zl")
    group_grad = jnp.moveaxis(groups, 0, 1).reshape(tokens, KV * HEAD_DIM)
    increment = lax.dot_general(
        group_grad, value_proj[0], (((1,), (1,)), ((), ())), preferred_element_type=jnp.float32
    )
    residual_grad = (grad_in[0].astype(jnp.float32) + increment).astype(jnp.bfloat16)
    target_row = increment.astype(jnp.bfloat16)
    mine = lax.all_gather(target_row, PLANE, axis=0, tiled=False)
    delta = lax.all_to_all(pieces, TP, 0, 0, tiled=True)
    core = lax.axis_index("core")
    theirs = lax.ppermute(mine, "core", [(0, 1), (1, 0)])
    all_heads = delta.reshape(HEADS, tokens, local_width)
    contract = (((1, 2), (1, 2)), ((), ()))
    both = jnp.concatenate([mine, theirs], axis=0)
    scores = lax.dot_general(all_heads, both, contract, preferred_element_type=jnp.float32)
    half = scores.shape[1] // 2
    first = jnp.where(core == 0, scores[:, :half], scores[:, half:])
    second = jnp.where(core == 0, scores[:, half:], scores[:, :half])
    partial_scores = jnp.stack([first, second], axis=-1).reshape(HEADS, section_count)
    totals = from_everyone(partial_scores, TP).sum(axis=0)
    later = jnp.arange(section_count) > lax.axis_index(SECTION)
    raw_scores = jnp.where(later[None, :], totals / tokens, jnp.zeros_like(totals))
    onehot = (node_map[0][:, None] == jnp.arange(HEADS)[None, :]).astype(jnp.float32)
    edge_scores = jnp.dot(onehot.T, raw_scores, precision=lax.Precision.HIGHEST)
    return (residual_grad[None], edge_scores[None])


def solution(mesh):
    sections, tps = mesh.devices.shape
    side = int(round(np.sqrt(tps)))
    cores = 2
    rows = int(round(np.sqrt(sections // cores)))
    fine = Mesh(
        mesh.devices.reshape(sections // cores // rows, rows, cores, tps // side, side),
        SECTION + TP,
    )
    placed = (
        P(SECTION, None, TP),
        P(SECTION, TP, None),
        P(SECTION, TP, None),
        P(SECTION, None, TP),
        P(SECTION, TP, None, None),
        P(),
        P(SECTION, None),
    )
    return jax.shard_map(
        on_device,
        mesh=fine,
        in_specs=placed,
        out_specs=(P(SECTION, None, TP), P(SECTION, None, None)),
        check_vma=False,
    )
```

```python
import jax
import jax.numpy as jnp
import numpy as np
from jax import lax
from jax.sharding import Mesh
from jax.sharding import PartitionSpec as P

HEADS = 32
HEAD_DIM = 128
KV = 4
PROMPT = 32
GROUP = 8
TP = ("zl", "x")
SECTION = ("zh", "y", "core")
PLANE = ("zh", "y")


def from_everyone(array, axis):
    count = lax.axis_size(axis)
    return lax.all_to_all(
        jnp.broadcast_to(array[None], (count, *array.shape)), axis, 0, 0, tiled=True
    )


def on_device(grad_in, out_proj, value_proj, head_delta, pattern, positions, node_map):
    tokens = grad_in.shape[1]
    local_width = grad_in.shape[2]
    own_rows = out_proj.shape[1]
    own_heads = own_rows // HEAD_DIM
    width = out_proj.shape[2]
    tp_count = lax.axis_size(TP)
    section_count = lax.axis_size(SECTION)
    weights = out_proj[0]

    own_delta = jnp.einsum(
        "thc,hcd->htd",
        head_delta[0].reshape(tokens, own_heads, HEAD_DIM),
        weights.reshape(own_heads, HEAD_DIM, width),
        preferred_element_type=jnp.float32,
    ).astype(jnp.bfloat16)
    pieces = own_delta.reshape(own_heads, tokens, tp_count, local_width).transpose(2, 0, 1, 3)

    token_ids = jnp.arange(tokens)
    block_ids = token_ids // PROMPT
    allowed = (
        (block_ids[:, None] == block_ids[None, :])
        & (positions[None, :] >= 0)
        & (positions[None, :] <= positions[:, None])
    )
    visible = allowed.astype(jnp.bfloat16)
    column = from_everyone(grad_in[0], "zl")
    pieces, column = lax.optimization_barrier((pieces, column))
    row = from_everyone(column, "x")
    grad_rows = jnp.transpose(row, (2, 1, 0, 3)).reshape(tokens, width)
    head_grad = lax.dot_general(
        grad_rows,
        weights,
        (((1,), (1,)), ((), ())),
        preferred_element_type=jnp.float32,
    ).astype(jnp.bfloat16)
    masked = pattern[0] * visible[None]
    value_grad = jnp.einsum(
        "hts,thc->shc",
        masked,
        head_grad.reshape(tokens, own_heads, HEAD_DIM),
        preferred_element_type=jnp.float32,
    ).astype(jnp.bfloat16)
    pair_sum = value_grad.astype(jnp.float32).sum(axis=1)
    group_sum = from_everyone(pair_sum, "x").sum(axis=0).astype(jnp.bfloat16)
    groups = from_everyone(group_sum, "zl")
    group_grad = jnp.moveaxis(groups, 0, 1).reshape(tokens, KV * HEAD_DIM)
    increment = lax.dot_general(
        group_grad, value_proj[0], (((1,), (1,)), ((), ())), preferred_element_type=jnp.float32
    )
    residual_grad = (grad_in[0].astype(jnp.float32) + increment).astype(jnp.bfloat16)
    target_row = increment.astype(jnp.bfloat16)
    mine = lax.all_gather(target_row, PLANE, axis=0, tiled=False)
    delta = lax.all_to_all(pieces, TP, 0, 0, tiled=True)
    core = lax.axis_index("core")
    theirs = lax.ppermute(mine, "core", [(0, 1), (1, 0)])
    all_heads = delta.reshape(HEADS, tokens, local_width)
    contract = (((1, 2), (1, 2)), ((), ()))
    both = jnp.concatenate([mine, theirs], axis=0)
    scores = lax.dot_general(all_heads, both, contract, preferred_element_type=jnp.float32)
    half = scores.shape[1] // 2
    first = jnp.where(core == 0, scores[:, :half], scores[:, half:])
    second = jnp.where(core == 0, scores[:, half:], scores[:, :half])
    partial_scores = jnp.stack([first, second], axis=-1).reshape(HEADS, section_count)
    totals = from_everyone(partial_scores, TP).sum(axis=0)
    later = jnp.arange(section_count) > lax.axis_index(SECTION)
    raw_scores = jnp.where(later[None, :], totals / tokens, jnp.zeros_like(totals))
    onehot = (node_map[0][:, None] == jnp.arange(HEADS)[None, :]).astype(jnp.float32)
    edge_scores = jnp.dot(onehot.T, raw_scores, precision=lax.Precision.HIGHEST)
    return (residual_grad[None], edge_scores[None])


def solution(mesh):
    sections, tps = mesh.devices.shape
    side = int(round(np.sqrt(tps)))
    cores = 2
    rows = int(round(np.sqrt(sections // cores)))
    fine = Mesh(
        mesh.devices.reshape(sections // cores // rows, rows, cores, tps // side, side),
        SECTION + TP,
    )
    placed = (
        P(SECTION, None, TP),
        P(SECTION, TP, None),
        P(SECTION, TP, None),
        P(SECTION, None, TP),
        P(SECTION, TP, None, None),
        P(),
        P(SECTION, None),
    )
    return jax.shard_map(
        on_device,
        mesh=fine,
        in_specs=placed,
        out_specs=(P(SECTION, None, TP), P(SECTION, None, None)),
        check_vma=False,
    )
```

```python
import jax
import jax.numpy as jnp
import numpy as np
from jax import lax
from jax.sharding import Mesh
from jax.sharding import PartitionSpec as P

HEADS = 32
HEAD_DIM = 128
KV = 4
PROMPT = 32
GROUP = 8
TP = ("zl", "x")
SECTION = ("zh", "y", "core")
PLANE = ("zh", "y")


def from_everyone(array, axis):
    count = lax.axis_size(axis)
    return lax.all_to_all(
        jnp.broadcast_to(array[None], (count, *array.shape)), axis, 0, 0, tiled=True
    )


def on_device(grad_in, out_proj, value_proj, head_delta, pattern, positions, node_map):
    tokens = grad_in.shape[1]
    local_width = grad_in.shape[2]
    own_rows = out_proj.shape[1]
    own_heads = own_rows // HEAD_DIM
    width = out_proj.shape[2]
    tp_count = lax.axis_size(TP)
    section_count = lax.axis_size(SECTION)
    weights = out_proj[0]

    blocks = weights.reshape(own_rows, tp_count, local_width).transpose(1, 0, 2)

    token_ids = jnp.arange(tokens)
    block_ids = token_ids // PROMPT
    allowed = (
        (block_ids[:, None] == block_ids[None, :])
        & (positions[None, :] >= 0)
        & (positions[None, :] <= positions[:, None])
    )
    visible = allowed.astype(jnp.bfloat16)
    both_cols = jnp.concatenate([grad_in[0], head_delta[0]], axis=1)
    column = from_everyone(both_cols, "zl")
    blocks, column = lax.optimization_barrier((blocks, column))
    row = jnp.transpose(from_everyone(column, "x"), (2, 1, 0, 3))
    grad_rows = row[..., :local_width].reshape(tokens, width)
    delta_cols = row[..., local_width:].reshape(tokens, HEADS * HEAD_DIM)
    head_grad = lax.dot_general(
        grad_rows,
        weights,
        (((1,), (1,)), ((), ())),
        preferred_element_type=jnp.float32,
    ).astype(jnp.bfloat16)
    masked = pattern[0] * visible[None]
    value_grad = jnp.einsum(
        "hts,thc->shc",
        masked,
        head_grad.reshape(tokens, own_heads, HEAD_DIM),
        preferred_element_type=jnp.float32,
    ).astype(jnp.bfloat16)
    pair_sum = value_grad.astype(jnp.float32).sum(axis=1)
    group_sum = from_everyone(pair_sum, "x").sum(axis=0).astype(jnp.bfloat16)
    groups = from_everyone(group_sum, "zl")
    group_grad = jnp.moveaxis(groups, 0, 1).reshape(tokens, KV * HEAD_DIM)
    increment = lax.dot_general(
        group_grad, value_proj[0], (((1,), (1,)), ((), ())), preferred_element_type=jnp.float32
    )
    residual_grad = (grad_in[0].astype(jnp.float32) + increment).astype(jnp.bfloat16)
    target_row = increment.astype(jnp.bfloat16)
    mine = lax.all_gather(target_row, PLANE, axis=0, tiled=False)
    column_blocks = lax.all_to_all(blocks, TP, 0, 0, tiled=True)
    core = lax.axis_index("core")
    theirs = lax.ppermute(mine, "core", [(0, 1), (1, 0)])
    all_heads = jnp.einsum(
        "thc,hcd->htd",
        delta_cols.reshape(tokens, HEADS, HEAD_DIM),
        column_blocks.reshape(HEADS, HEAD_DIM, local_width),
        preferred_element_type=jnp.float32,
    ).astype(jnp.bfloat16)
    contract = (((1, 2), (1, 2)), ((), ()))
    both = jnp.concatenate([mine, theirs], axis=0)
    scores = lax.dot_general(all_heads, both, contract, preferred_element_type=jnp.float32)
    half = scores.shape[1] // 2
    first = jnp.where(core == 0, scores[:, :half], scores[:, half:])
    second = jnp.where(core == 0, scores[:, half:], scores[:, :half])
    partial_scores = jnp.stack([first, second], axis=-1).reshape(HEADS, section_count)
    totals = from_everyone(partial_scores, TP).sum(axis=0)
    later = jnp.arange(section_count) > lax.axis_index(SECTION)
    raw_scores = jnp.where(later[None, :], totals / tokens, jnp.zeros_like(totals))
    onehot = (node_map[0][:, None] == jnp.arange(HEADS)[None, :]).astype(jnp.float32)
    edge_scores = jnp.dot(onehot.T, raw_scores, precision=lax.Precision.HIGHEST)
    return (residual_grad[None], edge_scores[None])


def solution(mesh):
    sections, tps = mesh.devices.shape
    side = int(round(np.sqrt(tps)))
    cores = 2
    rows = int(round(np.sqrt(sections // cores)))
    fine = Mesh(
        mesh.devices.reshape(sections // cores // rows, rows, cores, tps // side, side),
        SECTION + TP,
    )
    placed = (
        P(SECTION, None, TP),
        P(SECTION, TP, None),
        P(SECTION, TP, None),
        P(SECTION, None, TP),
        P(SECTION, TP, None, None),
        P(),
        P(SECTION, None),
    )
    return jax.shard_map(
        on_device,
        mesh=fine,
        in_specs=placed,
        out_specs=(P(SECTION, None, TP), P(SECTION, None, None)),
        check_vma=False,
    )
```

```python
import jax
import jax.numpy as jnp
import numpy as np
from jax import lax
from jax.sharding import Mesh
from jax.sharding import PartitionSpec as P

HEADS = 32
HEAD_DIM = 128
KV = 4
PROMPT = 32
GROUP = 8
TP = ("zl", "x")
SECTION = ("zh", "y", "core")


def from_everyone(array, axis):
    count = lax.axis_size(axis)
    return lax.all_to_all(
        jnp.broadcast_to(array[None], (count, *array.shape)), axis, 0, 0, tiled=True
    )


def on_device(grad_in, out_proj, value_proj, head_delta, pattern, positions, node_map):
    tokens = grad_in.shape[1]
    local_width = grad_in.shape[2]
    own_rows = out_proj.shape[1]
    own_heads = own_rows // HEAD_DIM
    width = out_proj.shape[2]
    tp_count = lax.axis_size(TP)
    section_count = lax.axis_size(SECTION)
    weights = out_proj[0]

    own_delta = jnp.einsum(
        "thc,hcd->htd",
        head_delta[0].reshape(tokens, own_heads, HEAD_DIM),
        weights.reshape(own_heads, HEAD_DIM, width),
        preferred_element_type=jnp.float32,
    ).astype(jnp.bfloat16)
    pieces = own_delta.reshape(own_heads, tokens, tp_count, local_width).transpose(2, 0, 1, 3)

    token_ids = jnp.arange(tokens)
    block_ids = token_ids // PROMPT
    allowed = (
        (block_ids[:, None] == block_ids[None, :])
        & (positions[None, :] >= 0)
        & (positions[None, :] <= positions[:, None])
    )
    visible = allowed.astype(jnp.bfloat16)
    column = from_everyone(grad_in[0], "zl")
    pieces, column = lax.optimization_barrier((pieces, column))
    row = from_everyone(column, "x")
    grad_rows = jnp.transpose(row, (2, 1, 0, 3)).reshape(tokens, width)
    head_grad = lax.dot_general(
        grad_rows,
        weights,
        (((1,), (1,)), ((), ())),
        preferred_element_type=jnp.float32,
    ).astype(jnp.bfloat16)
    masked = pattern[0] * visible[None]
    value_grad = jnp.einsum(
        "hts,thc->shc",
        masked,
        head_grad.reshape(tokens, own_heads, HEAD_DIM),
        preferred_element_type=jnp.float32,
    ).astype(jnp.bfloat16)
    pair_sum = value_grad.astype(jnp.float32).sum(axis=1)
    group_sum = from_everyone(pair_sum, "x").sum(axis=0).astype(jnp.bfloat16)
    groups = from_everyone(group_sum, "zl")
    group_grad = jnp.moveaxis(groups, 0, 1).reshape(tokens, KV * HEAD_DIM)
    increment = lax.dot_general(
        group_grad, value_proj[0], (((1,), (1,)), ((), ())), preferred_element_type=jnp.float32
    )
    residual_grad = (grad_in[0].astype(jnp.float32) + increment).astype(jnp.bfloat16)
    target_row = increment.astype(jnp.bfloat16)
    target_rows = lax.all_gather(target_row, SECTION, axis=0, tiled=False)
    delta = lax.all_to_all(pieces, TP, 0, 0, tiled=True)
    all_heads = delta.reshape(HEADS, tokens, local_width)
    contract = (((1, 2), (1, 2)), ((), ()))
    partial_scores = lax.dot_general(
        target_rows, all_heads, contract, preferred_element_type=jnp.float32
    ).T
    totals = from_everyone(partial_scores, TP).sum(axis=0)
    later = jnp.arange(section_count) > lax.axis_index(SECTION)
    raw_scores = jnp.where(later[None, :], totals / tokens, jnp.zeros_like(totals))
    onehot = (node_map[0][:, None] == jnp.arange(HEADS)[None, :]).astype(jnp.float32)
    edge_scores = jnp.dot(onehot.T, raw_scores, precision=lax.Precision.HIGHEST)
    return (residual_grad[None], edge_scores[None])


def solution(mesh):
    sections, tps = mesh.devices.shape
    side = int(round(np.sqrt(tps)))
    cores = 2
    rows = int(round(np.sqrt(sections // cores)))
    fine = Mesh(
        mesh.devices.reshape(sections // cores // rows, rows, cores, tps // side, side),
        SECTION + TP,
    )
    placed = (
        P(SECTION, None, TP),
        P(SECTION, TP, None),
        P(SECTION, TP, None),
        P(SECTION, None, TP),
        P(SECTION, TP, None, None),
        P(),
        P(SECTION, None),
    )
    return jax.shard_map(
        on_device,
        mesh=fine,
        in_specs=placed,
        out_specs=(P(SECTION, None, TP), P(SECTION, None, None)),
        check_vma=False,
    )
```

```python
import jax
import jax.numpy as jnp
import numpy as np
from jax import lax
from jax.sharding import Mesh
from jax.sharding import PartitionSpec as P

HEADS = 32
HEAD_DIM = 128
KV = 4
PROMPT = 32
GROUP = 8
TP = ("zl", "x")
SECTION = ("zh", "y", "core")
PLANE = ("zh", "y")


def from_everyone(array, axis):
    count = lax.axis_size(axis)
    return lax.all_to_all(
        jnp.broadcast_to(array[None], (count, *array.shape)), axis, 0, 0, tiled=True
    )


def on_device(grad_in, out_proj, value_proj, head_delta, pattern, positions, node_map):
    tokens = grad_in.shape[1]
    local_width = grad_in.shape[2]
    own_rows = out_proj.shape[1]
    own_heads = own_rows // HEAD_DIM
    width = out_proj.shape[2]
    tp_count = lax.axis_size(TP)
    section_count = lax.axis_size(SECTION)
    weights = out_proj[0]

    own_delta = jnp.einsum(
        "thc,hcd->htd",
        head_delta[0].reshape(tokens, own_heads, HEAD_DIM),
        weights.reshape(own_heads, HEAD_DIM, width),
        preferred_element_type=jnp.float32,
    ).astype(jnp.bfloat16)
    pieces = own_delta.reshape(own_heads, tokens, tp_count, local_width).transpose(2, 0, 1, 3)

    token_ids = jnp.arange(tokens)
    block_ids = token_ids // PROMPT
    allowed = (
        (block_ids[:, None] == block_ids[None, :])
        & (positions[None, :] >= 0)
        & (positions[None, :] <= positions[:, None])
    )
    visible = allowed.astype(jnp.bfloat16)
    column = from_everyone(grad_in[0], "zl")
    pieces, column = lax.optimization_barrier((pieces, column))
    row = from_everyone(column, "x")
    grad_rows = jnp.transpose(row, (2, 1, 0, 3)).reshape(tokens, width)
    head_grad = lax.dot_general(
        grad_rows,
        weights,
        (((1,), (1,)), ((), ())),
        preferred_element_type=jnp.float32,
    ).astype(jnp.bfloat16)
    masked = pattern[0] * visible[None]
    value_grad = jnp.einsum(
        "hts,thc->shc",
        masked,
        head_grad.reshape(tokens, own_heads, HEAD_DIM),
        preferred_element_type=jnp.float32,
    ).astype(jnp.bfloat16)
    pair_sum = value_grad.astype(jnp.float32).sum(axis=1)
    group_sum = from_everyone(pair_sum, "x").sum(axis=0).astype(jnp.bfloat16)
    groups = from_everyone(group_sum, "zl")
    group_grad = jnp.moveaxis(groups, 0, 1).reshape(tokens, KV * HEAD_DIM)
    increment = lax.dot_general(
        group_grad, value_proj[0], (((1,), (1,)), ((), ())), preferred_element_type=jnp.float32
    )
    residual_grad = (grad_in[0].astype(jnp.float32) + increment).astype(jnp.bfloat16)
    target_row = increment.astype(jnp.bfloat16)
    mine_flat = lax.all_gather(target_row, PLANE, axis=0, tiled=True)
    mine = mine_flat.reshape(-1, tokens, local_width)
    delta = lax.all_to_all(pieces, TP, 0, 0, tiled=True)
    core = lax.axis_index("core")
    theirs = lax.ppermute(mine_flat, "core", [(0, 1), (1, 0)]).reshape(mine.shape)
    all_heads = delta.reshape(HEADS, tokens, local_width)
    contract = (((1, 2), (1, 2)), ((), ()))
    both = jnp.concatenate([mine, theirs], axis=0)
    scores = lax.dot_general(all_heads, both, contract, preferred_element_type=jnp.float32)
    half = scores.shape[1] // 2
    first = jnp.where(core == 0, scores[:, :half], scores[:, half:])
    second = jnp.where(core == 0, scores[:, half:], scores[:, :half])
    partial_scores = jnp.stack([first, second], axis=-1).reshape(HEADS, section_count)
    totals = from_everyone(partial_scores, TP).sum(axis=0)
    later = jnp.arange(section_count) > lax.axis_index(SECTION)
    raw_scores = jnp.where(later[None, :], totals / tokens, jnp.zeros_like(totals))
    onehot = (node_map[0][:, None] == jnp.arange(HEADS)[None, :]).astype(jnp.float32)
    edge_scores = jnp.dot(onehot.T, raw_scores, precision=lax.Precision.HIGHEST)
    return (residual_grad[None], edge_scores[None])


def solution(mesh):
    sections, tps = mesh.devices.shape
    side = int(round(np.sqrt(tps)))
    cores = 2
    rows = int(round(np.sqrt(sections // cores)))
    fine = Mesh(
        mesh.devices.reshape(sections // cores // rows, rows, cores, tps // side, side),
        SECTION + TP,
    )
    placed = (
        P(SECTION, None, TP),
        P(SECTION, TP, None),
        P(SECTION, TP, None),
        P(SECTION, None, TP),
        P(SECTION, TP, None, None),
        P(),
        P(SECTION, None),
    )
    return jax.shard_map(
        on_device,
        mesh=fine,
        in_specs=placed,
        out_specs=(P(SECTION, None, TP), P(SECTION, None, None)),
        check_vma=False,
    )
```

```python
import jax
import jax.numpy as jnp
import numpy as np
from jax import lax
from jax.sharding import Mesh
from jax.sharding import PartitionSpec as P

HEADS = 32
HEAD_DIM = 128
KV = 4
PROMPT = 32
GROUP = 8
TP = ("zl", "x")
SECTION = ("zh", "y", "core")
PLANE = ("zh", "y")


def from_everyone(array, axis):
    count = lax.axis_size(axis)
    return lax.all_to_all(
        jnp.broadcast_to(array[None], (count, *array.shape)), axis, 0, 0, tiled=True
    )


def on_device(grad_in, out_proj, value_proj, head_delta, pattern, positions, node_map):
    tokens = grad_in.shape[1]
    local_width = grad_in.shape[2]
    own_rows = out_proj.shape[1]
    own_heads = own_rows // HEAD_DIM
    width = out_proj.shape[2]
    tp_count = lax.axis_size(TP)
    section_count = lax.axis_size(SECTION)
    weights = out_proj[0]

    own_delta = jnp.einsum(
        "thc,hcd->htd",
        head_delta[0].reshape(tokens, own_heads, HEAD_DIM),
        weights.reshape(own_heads, HEAD_DIM, width),
        preferred_element_type=jnp.float32,
    ).astype(jnp.bfloat16)
    pieces = own_delta.reshape(own_heads, tokens, tp_count, local_width).transpose(2, 0, 1, 3)

    token_ids = jnp.arange(tokens)
    block_ids = token_ids // PROMPT
    allowed = (
        (block_ids[:, None] == block_ids[None, :])
        & (positions[None, :] >= 0)
        & (positions[None, :] <= positions[:, None])
    )
    visible = allowed.astype(jnp.bfloat16)
    column = from_everyone(grad_in[0], "zl")
    pieces, column = lax.optimization_barrier((pieces, column))
    row = from_everyone(column, "x")
    zl_count = column.shape[0]
    by_block = weights.reshape(own_rows, zl_count, tp_count // zl_count, local_width)
    head_grad = jnp.einsum(
        "xztc,jzxc->tj", row, by_block, preferred_element_type=jnp.float32
    ).astype(jnp.bfloat16)
    masked = pattern[0] * visible[None]
    value_grad = jnp.einsum(
        "hts,thc->shc",
        masked,
        head_grad.reshape(tokens, own_heads, HEAD_DIM),
        preferred_element_type=jnp.float32,
    ).astype(jnp.bfloat16)
    pair_sum = value_grad.astype(jnp.float32).sum(axis=1)
    group_sum = from_everyone(pair_sum, "x").sum(axis=0).astype(jnp.bfloat16)
    groups = from_everyone(group_sum, "zl")
    group_grad = jnp.moveaxis(groups, 0, 1).reshape(tokens, KV * HEAD_DIM)
    increment = lax.dot_general(
        group_grad, value_proj[0], (((1,), (1,)), ((), ())), preferred_element_type=jnp.float32
    )
    residual_grad = (grad_in[0].astype(jnp.float32) + increment).astype(jnp.bfloat16)
    target_row = increment.astype(jnp.bfloat16)
    mine = lax.all_gather(target_row, PLANE, axis=0, tiled=False)
    delta = lax.all_to_all(pieces, TP, 0, 0, tiled=True)
    core = lax.axis_index("core")
    theirs = lax.ppermute(mine, "core", [(0, 1), (1, 0)])
    all_heads = delta.reshape(HEADS, tokens, local_width)
    contract = (((1, 2), (1, 2)), ((), ()))
    both = jnp.concatenate([mine, theirs], axis=0)
    scores = lax.dot_general(all_heads, both, contract, preferred_element_type=jnp.float32)
    half = scores.shape[1] // 2
    first = jnp.where(core == 0, scores[:, :half], scores[:, half:])
    second = jnp.where(core == 0, scores[:, half:], scores[:, :half])
    partial_scores = jnp.stack([first, second], axis=-1).reshape(HEADS, section_count)
    totals = from_everyone(partial_scores, TP).sum(axis=0)
    later = jnp.arange(section_count) > lax.axis_index(SECTION)
    raw_scores = jnp.where(later[None, :], totals / tokens, jnp.zeros_like(totals))
    onehot = (node_map[0][:, None] == jnp.arange(HEADS)[None, :]).astype(jnp.float32)
    edge_scores = jnp.dot(onehot.T, raw_scores, precision=lax.Precision.HIGHEST)
    return (residual_grad[None], edge_scores[None])


def solution(mesh):
    sections, tps = mesh.devices.shape
    side = int(round(np.sqrt(tps)))
    cores = 2
    rows = int(round(np.sqrt(sections // cores)))
    fine = Mesh(
        mesh.devices.reshape(sections // cores // rows, rows, cores, tps // side, side),
        SECTION + TP,
    )
    placed = (
        P(SECTION, None, TP),
        P(SECTION, TP, None),
        P(SECTION, TP, None),
        P(SECTION, None, TP),
        P(SECTION, TP, None, None),
        P(),
        P(SECTION, None),
    )
    return jax.shard_map(
        on_device,
        mesh=fine,
        in_specs=placed,
        out_specs=(P(SECTION, None, TP), P(SECTION, None, None)),
        check_vma=False,
    )
```
